256 devices in a mesh: win: 32 (over x, y, core), exp: 8 (over z).
Axes of the slice: x: 4, y: 4, z: 8, core: 2. Of those that a mesh axis runs over, the one named last changes fastest.
Arguments:
- tokens: bfloat16 [16384, 2048], P('win'), may hold values from -9 to 9
- router: bfloat16 [2048, 32], replicated, may hold values from -0.125 to 0.125
- w_in: bfloat16 [32, 2048, 8192], P('win', None, 'exp'), may hold values from -0.125 to 0.125
- w_out: bfloat16 [32, 8192, 2048], P('win', 'exp'), may hold values from -0.0625 to 0.0625
- expert_ids: int32 [16384, 2], P('win'), may hold values from 0 to 31, all different within a row; in each aligned block of 512 rows (0 to 511, 512 to 1023, ...) at most 48 rows name the same one
- offsets: int32 [32], P('win'), may hold values from 0 to 63
Outputs:
- consensus_state: bfloat16 [16384, 2048], P('win', 'exp')
The draws below stay inside these ranges and needn't reach their ends.
Inputs may be any that keep to these rules, and one draw needn't show every extreme that they name: `expert_ids`: in each window (an aligned block of 512 rows) no expert is named by more than 48 choices, a bound that some block reaches; a token's two experts differ.
All inputs are finite; a program needn't handle non-finite values.
Results may differ from the reference program's by a relative error of at most 0.015.
Values may be sent and summed in bfloat16 or wider, within the bound.
No kernel may reach another device: no remote copies, remote signals or barrier semaphores. Data moves between devices by JAX's collectives and lax.ppermute only.
A program may use at most 128 MiB of HBM per device.

```python
import math
import jax
import jax.numpy as jnp
import numpy as np
from jax import lax

D = 2048
FF = 8192
EXPERTS = 32
T_DEV = 512
OV = 256
CAP = 48
WINDOWS = 32
TOKENS = 16384


def draw_tokens(key, part):
    base = jnp.clip(jax.random.normal(key, (WINDOWS, T_DEV, D), jnp.float32), -6.0, 6.0)
    return base.reshape(TOKENS, D).astype(jnp.bfloat16)


def touch_ends(result, own_key, least, top_value):
    place = [jax.random.randint(jax.random.fold_in(own_key, axis), (), 0, length) for axis, length in enumerate(result.shape)]
    main_axis = result.shape.index(max(result.shape))
    next_to = place[:main_axis] + [(place[main_axis] + 1) % result.shape[main_axis]] + place[main_axis + 1:]
    return result.at[tuple(place)].set(least).at[tuple(next_to)].set(top_value)


def shard_levels(stream_key, shape, shards, least, largest):
    loudness = 1.0
    for dim, blocks in shards:
        steps = jax.random.uniform(jax.random.fold_in(jax.random.fold_in(stream_key, 6), dim), (blocks,), jnp.float32, least / len(shards), largest / len(shards))
        loudness = loudness * jnp.repeat(jnp.exp(steps), shape[dim] // blocks).reshape((-1,) + (1,) * (len(shape) - 1 - dim))
    return loudness


def shared_out(stream_key, own, number, rows, amount, top, bound, lean):
    ranking = jax.random.permutation(stream_key, amount)
    packed, ordinary = portions_of(amount, rows * top, bound, lean, True), portions_of(amount, rows * top, bound, lean, False)
    places = jnp.arange(amount)

    def named(tallies, offset_by):
        used = int((tallies > 0).sum())
        fixed = max(1, used // 4)
        moved = fixed + (places - fixed + offset_by * (used - fixed)) % max(1, amount - fixed)
        return jnp.zeros((amount,), jnp.int32).at[ranking[jnp.where(places < fixed, places, moved)]].set(jnp.asarray(tallies, jnp.int32))

    tallies = jnp.where(number % 4 == 0, named(packed, number // 4), named(ordinary, number - number // 4 - 1))
    mixed = jax.random.permutation(jax.random.fold_in(own, 3), amount)
    donor, sink = mixed[0:amount // 2 * 2:2], mixed[1:amount // 2 * 2:2]
    slack = jnp.minimum(tallies[donor] - 1, bound - tallies[sink]) // 2
    slack = jnp.where((donor == ranking[0]) | (sink == ranking[0]) | (tallies[sink] == 0), 0, jnp.maximum(slack, 0))
    moved = jax.random.randint(jax.random.fold_in(own, 4), (amount // 2,), 0, 1 << 20) % (slack + 1)
    tallies = tallies.at[donor].add(-moved).at[sink].add(moved)
    members = jnp.searchsorted(jnp.cumsum(tallies), jnp.arange(rows * top), side="right").astype(jnp.int32)
    listing = members.reshape(top, rows).T
    listing = listing[jax.random.permutation(jax.random.fold_in(own, 1), rows)]
    offset_by = jax.random.randint(jax.random.fold_in(own, 2), (rows, 1), 0, top)
    return jnp.take_along_axis(listing, (jnp.arange(top)[None, :] + offset_by) % top, axis=1)


def portions_of(amount, total, limit, lean, full):
    portions = [(1 << 20) // math.isqrt(standing ** lean) + 1 for standing in range(1, amount + 1)]
    largest = limit if full else min(limit, max(-(-total // amount), total * portions[0] // sum(portions)))
    least = 1 if total - largest >= amount - 1 else 0
    holding, spare = [largest] + [least] * (amount - 1), total - largest - least * (amount - 1)
    while spare > 0:
        free = [i for i in range(1, amount) if holding[i] < largest] or [i for i in range(1, amount) if holding[i] < limit]
        mass, budget = sum([portions[i] for i in free]), spare
        for i in free:
            addition = min(limit - holding[i], max(1, budget * portions[i] // mass), spare)
            holding[i] = holding[i] + addition
            spare = spare - addition
    return np.array(holding)


def gaussian(key, extent, scale, bound, split=(), kind=jnp.bfloat16):
    entries = jax.random.normal(key, extent, jnp.float32) * scale
    if len(split) > 0:
        entries = shard_levels(key, extent, split, -0.22, 0.18) * entries
    return jnp.clip(entries, min=-bound, max=bound).astype(kind)


def setup_inputs(seed: int = 0) -> dict:
    streams_of = jax.random.split(jax.random.key(seed), 7)
    tokens = draw_tokens(jax.random.fold_in(streams_of[6], 71), 0)
    router = gaussian(streams_of[1], (D, EXPERTS), D ** -0.5, 0.125)
    w_in = gaussian(streams_of[2], (EXPERTS, D, FF), D ** -0.5, 0.125, ((0, 32), (2, 8)))
    w_out = gaussian(streams_of[3], (EXPERTS, FF, D), FF ** -0.5, 0.0625, ((0, 32), (1, 8)))
    expert_ids_keys = jax.random.split(jax.random.fold_in(streams_of[4], 1), TOKENS // T_DEV)
    expert_ids_turns = jax.random.permutation(jax.random.fold_in(streams_of[4], 3), TOKENS // T_DEV)
    expert_ids = jax.vmap(lambda own, number: shared_out(jax.random.fold_in(streams_of[4], 2), own, number, T_DEV, EXPERTS, 2, CAP, 1))(expert_ids_keys, expert_ids_turns).reshape((TOKENS, 2))
    offsets = touch_ends(jax.random.randint(streams_of[5], (WINDOWS,), 0, OV // 4), jax.random.fold_in(streams_of[5], 1), 0, (OV // 4) - 1).astype(jnp.int32)
    return dict(tokens=tokens, router=router, w_in=w_in, w_out=w_out, expert_ids=expert_ids, offsets=offsets)


def slot_numbers(flat_ids):
    expert_order = jnp.arange(EXPERTS, dtype=jnp.int32)
    hit_table = (flat_ids[:, None] == expert_order[None, :]).astype(jnp.int32)
    rank_table = jnp.cumsum(hit_table, axis=0) - 1
    return lax.optimization_barrier(jnp.sum(hit_table * rank_table, axis=1)).astype(jnp.int32)

def source_rows(slot_target):
    token_index = jnp.repeat(jnp.arange(T_DEV, dtype=jnp.int32), 2)
    return jnp.full((EXPERTS * CAP,), T_DEV, jnp.int32).at[slot_target].set(token_index)

def expert_apply(operands):
    rows_in, first_proj, second_proj = operands
    hidden_rows = jax.nn.relu(jnp.dot(rows_in, first_proj, preferred_element_type=jnp.float32)).astype(jnp.bfloat16)
    return jnp.dot(hidden_rows, second_proj, preferred_element_type=jnp.float32)

def reference(tokens, router, w_in, w_out, expert_ids, offsets):
    windowed = tokens.reshape(WINDOWS, T_DEV, D)
    flat_ids = expert_ids.reshape(WINDOWS, T_DEV * 2).astype(jnp.int32)
    slot_index = jax.vmap(slot_numbers)(flat_ids)
    slot_target = (flat_ids * CAP + slot_index).astype(jnp.int32)
    source_table = jax.vmap(source_rows)(slot_target)
    padded = jnp.concatenate([windowed, jnp.zeros((WINDOWS, 1, D), tokens.dtype)], axis=1)
    dispatched = jax.vmap(lambda rows_all, table_one: rows_all[table_one])(padded, source_table)
    dispatched = dispatched.reshape(WINDOWS, EXPERTS, CAP, D).transpose(1, 0, 2, 3).reshape(EXPERTS, WINDOWS * CAP, D)
    expert_out = lax.map(expert_apply, (dispatched, w_in, w_out))
    expert_out = expert_out.reshape(EXPERTS, WINDOWS, CAP, D).transpose(1, 0, 2, 3).reshape(WINDOWS, EXPERTS * CAP, D)
    logits = jnp.dot(tokens, router, preferred_element_type=jnp.float32).reshape(WINDOWS, T_DEV, EXPERTS)
    chosen = jnp.take_along_axis(logits, expert_ids.reshape(WINDOWS, T_DEV, 2), axis=2)
    gate_first = jax.nn.sigmoid(chosen[:, :, 0:1] - chosen[:, :, 1:2])
    gate_second = jax.nn.sigmoid(chosen[:, :, 1:2] - chosen[:, :, 0:1])
    picked = jax.vmap(lambda rows_all, index_one: rows_all[index_one])(expert_out, slot_target)
    picked = picked.reshape(WINDOWS, T_DEV, 2, D)
    layer_state = (windowed.astype(jnp.float32) + (gate_first * picked[:, :, 0] + gate_second * picked[:, :, 1])).astype(jnp.bfloat16)
    head_rows = layer_state[1:, :OV].astype(jnp.float32)
    previous = layer_state[:-1, T_DEV - OV:].astype(jnp.float32)
    scores = jnp.einsum('wid,wjd->wij', head_rows, previous, precision=lax.Precision.HIGHEST)
    row_pos = jnp.arange(OV, dtype=jnp.int32)[None, :, None]
    col_pos = jnp.arange(OV, dtype=jnp.int32)[None, None, :]
    distance = jnp.abs(col_pos - row_pos - offsets[1:].astype(jnp.int32)[:, None, None]).astype(jnp.float32) * (8.0 / OV)
    scores = scores / math.sqrt(D) - distance
    weights = jax.nn.softmax(scores, axis=-1).astype(jnp.bfloat16)
    blended = jnp.einsum('wij,wjd->wid', weights.astype(jnp.float32), previous, precision=lax.Precision.HIGHEST)
    mixed_rows = (0.5 * (head_rows + blended)).astype(jnp.bfloat16)
    consensus = layer_state.at[1:, :OV].set(mixed_rows)
    return consensus.reshape(TOKENS, D)
```

```python
import math

import jax
import jax.numpy as jnp
from jax import lax
from jax.sharding import PartitionSpec as P

D = 2048
EXPERTS = 32
OV = 256
CAP = 48


def shifted(shard, axis, by):
    count = lax.axis_size(axis)
    pairs = [(i, i + by) for i in range(count) if 0 <= i + by < count]
    return lax.ppermute(shard, axis, pairs)


def ring_reduce(blocks, axis, step):
    count = blocks.shape[1]
    me = lax.axis_index(axis)
    perm = [(i, (i + step) % count) for i in range(count)]

    def take(k):
        idx = (me - step * k + 2 * count) % count
        return lax.dynamic_index_in_dim(blocks, idx, axis=1, keepdims=False)

    acc = take(1)
    for k in range(count - 1):
        recv = lax.ppermute(acc.astype(jnp.bfloat16), axis, perm)
        acc = recv.astype(jnp.float32) + take(k + 2)
    return acc


def tree_sum(x, axis):
    count = lax.axis_size(axis)
    span = 1
    while span < count:
        x = x + lax.ppermute(x, axis, [(i, i ^ span) for i in range(count)])
        span *= 2
    return x


def shards(tokens, router, w_in, w_out, expert_ids, offsets):
    tok_count = tokens.shape[0]
    win_size = lax.axis_size("win")
    exp_size = lax.axis_size("exp")
    local_experts = w_in.shape[0]
    col_width = D // exp_size
    flat_ids = expert_ids.reshape(-1)
    expert_order = jnp.arange(EXPERTS, dtype=jnp.int32)
    hit_table = (flat_ids[:, None] == expert_order[None, :]).astype(jnp.int32)
    rank_table = jnp.cumsum(hit_table, axis=0) - 1
    slot_index = jnp.sum(hit_table * rank_table, axis=1)
    slot_target = flat_ids * CAP + slot_index
    token_index = jnp.repeat(jnp.arange(tok_count, dtype=jnp.int32), 2)
    source_table = jnp.full((EXPERTS * CAP,), tok_count, jnp.int32).at[slot_target].set(token_index)
    padded = jnp.concatenate([tokens, jnp.zeros((1, D), tokens.dtype)], axis=0)
    outgoing = padded[source_table].reshape(win_size, local_experts, CAP, D)
    arrived = lax.all_to_all(outgoing, "win", split_axis=0, concat_axis=0, tiled=True)
    hidden_rows = jnp.einsum(
        "secd,edf->secf", arrived, w_in, preferred_element_type=jnp.float32
    )
    hidden_rows = jax.nn.relu(hidden_rows).astype(jnp.bfloat16)
    results = jnp.einsum("secf,efd->secd", hidden_rows, w_out, preferred_element_type=jnp.float32)
    half = col_width // 2
    blocks = results.reshape(win_size * local_experts * CAP, exp_size, 2, half)
    reduced = jnp.concatenate(
        [ring_reduce(blocks[:, :, 0], "exp", 1), ring_reduce(blocks[:, :, 1], "exp", -1)], axis=-1
    )
    reduced = reduced.reshape(win_size, local_experts * CAP, col_width)
    returned = lax.all_to_all(reduced, "win", split_axis=0, concat_axis=0, tiled=True)
    logits = jnp.dot(tokens, router, preferred_element_type=jnp.float32)
    first_hit = expert_ids[:, 0:1] == expert_order[None, :]
    second_hit = expert_ids[:, 1:2] == expert_order[None, :]
    logit_first = jnp.sum(jnp.where(first_hit, logits, 0.0), axis=1, keepdims=True)
    logit_second = jnp.sum(jnp.where(second_hit, logits, 0.0), axis=1, keepdims=True)
    gate_first = jax.nn.sigmoid(logit_first - logit_second)
    gate_second = jax.nn.sigmoid(logit_second - logit_first)
    flat_rows = returned.reshape(EXPERTS * CAP, col_width)
    picked = flat_rows[slot_target].reshape(tok_count, 2, col_width)
    expert_sum = gate_first * picked[:, 0] + gate_second * picked[:, 1]
    own_cols = lax.dynamic_slice_in_dim(tokens, lax.axis_index("exp") * col_width, col_width, 1)
    layer_state = (own_cols.astype(jnp.float32) + expert_sum).astype(jnp.bfloat16)
    head_rows = layer_state[:OV]
    tail_rows = layer_state[tok_count - OV :]
    previous = shifted(tail_rows, "win", 1)
    contract = (((1,), (1,)), ((), ()))
    partial_scores = lax.dot_general(
        head_rows, previous, contract, preferred_element_type=jnp.float32
    )
    scores = tree_sum(partial_scores, "exp")
    row_pos = jnp.arange(OV, dtype=jnp.int32)[:, None]
    col_pos = jnp.arange(OV, dtype=jnp.int32)[None, :]
    distance = jnp.abs(col_pos - row_pos - offsets[0]).astype(jnp.float32) * (8.0 / OV)
    scores = scores / math.sqrt(D) - distance
    weights = jax.nn.softmax(scores, axis=-1).astype(jnp.bfloat16)
    blended = jnp.dot(weights, previous, preferred_element_type=jnp.float32)
    mixed_rows = (0.5 * (head_rows.astype(jnp.float32) + blended)).astype(jnp.bfloat16)
    mixed_rows = jnp.where(lax.axis_index("win") > 0, mixed_rows, head_rows)
    return jnp.concatenate([mixed_rows, layer_state[OV:]], axis=0)


def solution(mesh):
    return jax.shard_map(
        shards,
        mesh=mesh,
        in_specs=(
            P("win", None),
            P(),
            P("win", None, "exp"),
            P("win", "exp", None),
            P("win", None),
            P("win"),
        ),
        out_specs=P("win", "exp"),
        check_vma=False,
    )
```

```python
import math

import jax
import jax.numpy as jnp
from jax import lax
from jax.sharding import PartitionSpec as P

D = 2048
EXPERTS = 32
OV = 256
CAP = 48


def shifted(shard, axis, by):
    count = lax.axis_size(axis)
    pairs = [(i, i + by) for i in range(count) if 0 <= i + by < count]
    return lax.ppermute(shard, axis, pairs)


def ring_reduce(rows, weight, axis, step, half):
    count = lax.axis_size(axis)
    me = lax.axis_index(axis)
    perm = [(i, (i + step) % count) for i in range(count)]
    part = 0 if step > 0 else 1

    def take(k):
        block = (me - step * k + 2 * count) % count
        cols = lax.dynamic_slice_in_dim(weight, (block * 2 + part) * half, half, axis=1)
        return jnp.dot(rows, cols, preferred_element_type=jnp.float32)

    acc = take(1)
    for k in range(count - 1):
        recv = lax.ppermute(acc.astype(jnp.bfloat16), axis, perm)
        acc = recv.astype(jnp.float32) + take(k + 2)
    return acc


def tree_sum(x, axis):
    count = lax.axis_size(axis)
    span = 1
    while span < count:
        x = x + lax.ppermute(x, axis, [(i, i ^ span) for i in range(count)])
        span *= 2
    return x


def shards(tokens, router, w_in, w_out, expert_ids, offsets):
    tok_count = tokens.shape[0]
    win_size = lax.axis_size("win")
    exp_size = lax.axis_size("exp")
    local_experts = w_in.shape[0]
    col_width = D // exp_size
    flat_ids = expert_ids.reshape(-1)
    expert_order = jnp.arange(EXPERTS, dtype=jnp.int32)
    hit_table = (flat_ids[:, None] == expert_order[None, :]).astype(jnp.bfloat16)
    choice_pos = jnp.arange(flat_ids.shape[0], dtype=jnp.int32)
    lower = (choice_pos[:, None] >= choice_pos[None, :]).astype(jnp.bfloat16)
    rank_table = jnp.dot(lower, hit_table, preferred_element_type=jnp.float32)
    slot_index = (jnp.sum(hit_table.astype(jnp.float32) * rank_table, axis=1) - 1.0).astype(jnp.int32)
    slot_target = flat_ids * CAP + slot_index
    slot_pairs = slot_target.reshape(tok_count, 2)
    slot_order = jnp.arange(EXPERTS * CAP, dtype=jnp.int32)[None, :]
    chooser = ((slot_pairs[:, 0:1] == slot_order) | (slot_pairs[:, 1:2] == slot_order)).astype(tokens.dtype)
    outgoing = jnp.einsum("ts,td->sd", chooser, tokens, preferred_element_type=jnp.float32)
    outgoing = outgoing.astype(tokens.dtype).reshape(win_size, local_experts, CAP, D)
    arrived = lax.all_to_all(outgoing, "win", split_axis=0, concat_axis=0, tiled=True)
    hidden_rows = jnp.einsum(
        "secd,edf->secf", arrived, w_in, preferred_element_type=jnp.float32
    )
    hidden_rows = jax.nn.relu(hidden_rows).astype(jnp.bfloat16)
    half = col_width // 2
    rows = hidden_rows.reshape(win_size * local_experts * CAP, hidden_rows.shape[-1])
    weight = w_out.reshape(w_out.shape[-2], D)
    reduced = jnp.concatenate(
        [ring_reduce(rows, weight, "exp", 1, half), ring_reduce(rows, weight, "exp", -1, half)], axis=-1
    )
    reduced = reduced.reshape(win_size, local_experts * CAP, col_width)
    returned = lax.all_to_all(reduced, "win", split_axis=0, concat_axis=0, tiled=True)
    logits = jnp.dot(tokens, router, preferred_element_type=jnp.float32)
    first_hit = expert_ids[:, 0:1] == expert_order[None, :]
    second_hit = expert_ids[:, 1:2] == expert_order[None, :]
    logit_first = jnp.sum(jnp.where(first_hit, logits, 0.0), axis=1, keepdims=True)
    logit_second = jnp.sum(jnp.where(second_hit, logits, 0.0), axis=1, keepdims=True)
    gate_first = jax.nn.sigmoid(logit_first - logit_second)
    gate_second = jax.nn.sigmoid(logit_second - logit_first)
    flat_rows = returned.reshape(EXPERTS * CAP, col_width)
    picked = flat_rows[slot_target].reshape(tok_count, 2, col_width)
    expert_sum = gate_first * picked[:, 0] + gate_second * picked[:, 1]
    own_cols = lax.dynamic_slice_in_dim(tokens, lax.axis_index("exp") * col_width, col_width, 1)
    layer_state = (own_cols.astype(jnp.float32) + expert_sum).astype(jnp.bfloat16)
    head_rows = layer_state[:OV]
    tail_rows = layer_state[tok_count - OV :]
    previous = shifted(tail_rows, "win", 1)
    contract = (((1,), (1,)), ((), ()))
    partial_scores = lax.dot_general(
        head_rows, previous, contract, preferred_element_type=jnp.float32
    )
    scores = tree_sum(partial_scores, "exp")
    row_pos = jnp.arange(OV, dtype=jnp.int32)[:, None]
    col_pos = jnp.arange(OV, dtype=jnp.int32)[None, :]
    distance = jnp.abs(col_pos - row_pos - offsets[0]).astype(jnp.float32) * (8.0 / OV)
    scores = scores / math.sqrt(D) - distance
    weights = jax.nn.softmax(scores, axis=-1).astype(jnp.bfloat16)
    blended = jnp.dot(weights, previous, preferred_element_type=jnp.float32)
    mixed_rows = (0.5 * (head_rows.astype(jnp.float32) + blended)).astype(jnp.bfloat16)
    mixed_rows = jnp.where(lax.axis_index("win") > 0, mixed_rows, head_rows)
    return jnp.concatenate([mixed_rows, layer_state[OV:]], axis=0)


def solution(mesh):
    return jax.shard_map(
        shards,
        mesh=mesh,
        in_specs=(
            P("win", None),
            P(),
            P("win", None, "exp"),
            P("win", "exp", None),
            P("win", None),
            P("win"),
        ),
        out_specs=P("win", "exp"),
        check_vma=False,
    )
```

```python
import math

import jax
import jax.numpy as jnp
from jax import lax
from jax.sharding import PartitionSpec as P

D = 2048
EXPERTS = 32
OV = 256
CAP = 48
CHUNKS = 2


def shifted(shard, axis, by):
    count = lax.axis_size(axis)
    pairs = [(i, i + by) for i in range(count) if 0 <= i + by < count]
    return lax.ppermute(shard, axis, pairs)


def ring_reduce(rows, weight, axis, step, half):
    count = lax.axis_size(axis)
    me = lax.axis_index(axis)
    perm = [(i, (i + step) % count) for i in range(count)]
    part = 0 if step > 0 else 1

    def take(k):
        block = (me - step * k + 2 * count) % count
        cols = lax.dynamic_slice_in_dim(weight, (block * 2 + part) * half, half, axis=1)
        return jnp.dot(rows, cols, preferred_element_type=jnp.float32)

    acc = take(1)
    for k in range(count - 1):
        recv = lax.ppermute(acc.astype(jnp.bfloat16), axis, perm)
        acc = recv.astype(jnp.float32) + take(k + 2)
    return acc


def tree_sum(x, axis):
    count = lax.axis_size(axis)
    span = 1
    while span < count:
        x = x + lax.ppermute(x, axis, [(i, i ^ span) for i in range(count)])
        span *= 2
    return x


def shards(tokens, router, w_in, w_out, expert_ids, offsets):
    tok_count = tokens.shape[0]
    win_size = lax.axis_size("win")
    exp_size = lax.axis_size("exp")
    local_experts = w_in.shape[0]
    col_width = D // exp_size
    flat_ids = expert_ids.reshape(-1)
    expert_order = jnp.arange(EXPERTS, dtype=jnp.int32)
    hit_table = (flat_ids[:, None] == expert_order[None, :]).astype(jnp.bfloat16)
    choice_pos = jnp.arange(flat_ids.shape[0], dtype=jnp.int32)
    lower = (choice_pos[:, None] >= choice_pos[None, :]).astype(jnp.bfloat16)
    rank_table = jnp.dot(lower, hit_table, preferred_element_type=jnp.float32)
    slot_index = (jnp.sum(hit_table.astype(jnp.float32) * rank_table, axis=1) - 1.0).astype(jnp.int32)
    slot_target = flat_ids * CAP + slot_index
    slot_pairs = slot_target.reshape(tok_count, 2)
    half = col_width // 2
    weight = w_out.reshape(w_out.shape[-2], D)
    pieces = []
    for part in range(CHUNKS):
        width = CAP // CHUNKS
        slot_order = (
            jnp.arange(EXPERTS, dtype=jnp.int32)[:, None] * CAP
            + part * width
            + jnp.arange(width, dtype=jnp.int32)[None, :]
        ).reshape(1, -1)
        chooser = ((slot_pairs[:, 0:1] == slot_order) | (slot_pairs[:, 1:2] == slot_order)).astype(tokens.dtype)
        outgoing = jnp.einsum("ts,td->sd", chooser, tokens, preferred_element_type=jnp.float32)
        outgoing = outgoing.astype(tokens.dtype).reshape(win_size, local_experts, width, D)
        arrived = lax.all_to_all(outgoing, "win", split_axis=0, concat_axis=0, tiled=True)
        if pieces:
            arrived, _ = lax.optimization_barrier((arrived, reduced))
        hidden_rows = jnp.einsum("secd,edf->secf", arrived, w_in, preferred_element_type=jnp.float32)
        hidden_rows = jax.nn.relu(hidden_rows).astype(jnp.bfloat16)
        rows = hidden_rows.reshape(win_size * local_experts * width, hidden_rows.shape[-1])
        reduced = jnp.concatenate(
            [ring_reduce(rows, weight, "exp", 1, half), ring_reduce(rows, weight, "exp", -1, half)], axis=-1
        )
        reduced = reduced.reshape(win_size, local_experts * width, col_width)
        pieces.append(lax.all_to_all(reduced, "win", split_axis=0, concat_axis=0, tiled=True))
    returned = jnp.concatenate(pieces, axis=1)
    logits = jnp.dot(tokens, router, preferred_element_type=jnp.float32)
    first_hit = expert_ids[:, 0:1] == expert_order[None, :]
    second_hit = expert_ids[:, 1:2] == expert_order[None, :]
    logit_first = jnp.sum(jnp.where(first_hit, logits, 0.0), axis=1, keepdims=True)
    logit_second = jnp.sum(jnp.where(second_hit, logits, 0.0), axis=1, keepdims=True)
    gate_first = jax.nn.sigmoid(logit_first - logit_second)
    gate_second = jax.nn.sigmoid(logit_second - logit_first)
    flat_rows = returned.reshape(EXPERTS * CAP, col_width)
    picked = flat_rows[slot_target].reshape(tok_count, 2, col_width)
    expert_sum = gate_first * picked[:, 0] + gate_second * picked[:, 1]
    own_cols = lax.dynamic_slice_in_dim(tokens, lax.axis_index("exp") * col_width, col_width, 1)
    layer_state = (own_cols.astype(jnp.float32) + expert_sum).astype(jnp.bfloat16)
    head_rows = layer_state[:OV]
    tail_rows = layer_state[tok_count - OV :]
    previous = shifted(tail_rows, "win", 1)
    contract = (((1,), (1,)), ((), ()))
    partial_scores = lax.dot_general(
        head_rows, previous, contract, preferred_element_type=jnp.float32
    )
    scores = tree_sum(partial_scores, "exp")
    row_pos = jnp.arange(OV, dtype=jnp.int32)[:, None]
    col_pos = jnp.arange(OV, dtype=jnp.int32)[None, :]
    distance = jnp.abs(col_pos - row_pos - offsets[0]).astype(jnp.float32) * (8.0 / OV)
    scores = scores / math.sqrt(D) - distance
    weights = jax.nn.softmax(scores, axis=-1).astype(jnp.bfloat16)
    blended = jnp.dot(weights, previous, preferred_element_type=jnp.float32)
    mixed_rows = (0.5 * (head_rows.astype(jnp.float32) + blended)).astype(jnp.bfloat16)
    mixed_rows = jnp.where(lax.axis_index("win") > 0, mixed_rows, head_rows)
    return jnp.concatenate([mixed_rows, layer_state[OV:]], axis=0)


def solution(mesh):
    return jax.shard_map(
        shards,
        mesh=mesh,
        in_specs=(
            P("win", None),
            P(),
            P("win", None, "exp"),
            P("win", "exp", None),
            P("win", None),
            P("win"),
        ),
        out_specs=P("win", "exp"),
        check_vma=False,
    )
```

```python
import math

import jax
import jax.numpy as jnp
from jax import lax
from jax.sharding import PartitionSpec as P

D = 2048
EXPERTS = 32
OV = 256
CAP = 48


def shifted(shard, axis, by):
    count = lax.axis_size(axis)
    pairs = [(i, i + by) for i in range(count) if 0 <= i + by < count]
    return lax.ppermute(shard, axis, pairs)


def ring_reduce(rows, weight, axis, step, half):
    count = lax.axis_size(axis)
    me = lax.axis_index(axis)
    perm = [(i, (i + step) % count) for i in range(count)]
    part = 0 if step > 0 else 1

    def take(k):
        block = (me - step * k + 2 * count) % count
        cols = lax.dynamic_slice_in_dim(weight, (block * 2 + part) * half, half, axis=1)
        return jnp.dot(rows, cols, preferred_element_type=jnp.float32)

    acc = take(1)
    for k in range(count - 1):
        recv = lax.ppermute(acc.astype(jnp.bfloat16), axis, perm)
        acc = recv.astype(jnp.float32) + take(k + 2)
    return acc


def tree_sum(x, axis):
    count = lax.axis_size(axis)
    span = 1
    while span < count:
        x = x + lax.ppermute(x, axis, [(i, i ^ span) for i in range(count)])
        span *= 2
    return x


def shards(tokens, router, w_in, w_out, expert_ids, offsets):
    tok_count = tokens.shape[0]
    win_size = lax.axis_size("win")
    exp_size = lax.axis_size("exp")
    local_experts = w_in.shape[0]
    col_width = D // exp_size
    flat_ids = expert_ids.reshape(-1)
    expert_order = jnp.arange(EXPERTS, dtype=jnp.int32)
    hit_table = (flat_ids[:, None] == expert_order[None, :]).astype(jnp.bfloat16)
    choice_pos = jnp.arange(flat_ids.shape[0], dtype=jnp.int32)
    lower = (choice_pos[:, None] >= choice_pos[None, :]).astype(jnp.bfloat16)
    rank_table = jnp.dot(lower, hit_table, preferred_element_type=jnp.float32)
    slot_index = (jnp.sum(hit_table.astype(jnp.float32) * rank_table, axis=1) - 1.0).astype(jnp.int32)
    slot_target = flat_ids * CAP + slot_index
    slot_pairs = slot_target.reshape(tok_count, 2)
    slot_order = jnp.arange(EXPERTS * CAP, dtype=jnp.int32)[None, :]
    chooser = ((slot_pairs[:, 0:1] == slot_order) | (slot_pairs[:, 1:2] == slot_order)).astype(tokens.dtype)
    outgoing = jnp.einsum("ts,td->sd", chooser, tokens, preferred_element_type=jnp.float32)
    outgoing = outgoing.astype(tokens.dtype).reshape(win_size, local_experts, CAP, D)
    arrived = lax.all_to_all(outgoing, "win", split_axis=0, concat_axis=0, tiled=True)
    hidden_rows = jnp.einsum(
        "secd,edf->secf", arrived, w_in, preferred_element_type=jnp.float32
    )
    hidden_rows = jax.nn.relu(hidden_rows).astype(jnp.bfloat16)
    half = col_width // 2
    rows = hidden_rows.reshape(win_size * local_experts * CAP, hidden_rows.shape[-1])
    weight = w_out.reshape(w_out.shape[-2], D)
    reduced = jnp.concatenate(
        [ring_reduce(rows, weight, "exp", 1, half), ring_reduce(rows, weight, "exp", -1, half)], axis=-1
    )
    reduced = reduced.reshape(win_size, local_experts * CAP, col_width)
    returned = lax.all_to_all(reduced, "win", split_axis=0, concat_axis=0, tiled=True)
    logits = jnp.dot(tokens, router, preferred_element_type=jnp.float32)
    first_hit = expert_ids[:, 0:1] == expert_order[None, :]
    second_hit = expert_ids[:, 1:2] == expert_order[None, :]
    logit_first = jnp.sum(jnp.where(first_hit, logits, 0.0), axis=1, keepdims=True)
    logit_second = jnp.sum(jnp.where(second_hit, logits, 0.0), axis=1, keepdims=True)
    gate_first = jax.nn.sigmoid(logit_first - logit_second)
    gate_second = jax.nn.sigmoid(logit_second - logit_first)
    flat_rows = returned.reshape(EXPERTS * CAP, col_width)
    picked = flat_rows[slot_target].reshape(tok_count, 2, col_width)
    expert_sum = gate_first * picked[:, 0] + gate_second * picked[:, 1]
    own_cols = lax.dynamic_slice_in_dim(tokens, lax.axis_index("exp") * col_width, col_width, 1)
    layer_state = (own_cols.astype(jnp.float32) + expert_sum).astype(jnp.bfloat16)
    head_rows = layer_state[:OV]
    tail_rows = layer_state[tok_count - OV :]
    previous = shifted(tail_rows, "win", 1)
    contract = (((1,), (1,)), ((), ()))
    partial_scores = lax.dot_general(
        head_rows, previous, contract, preferred_element_type=jnp.float32
    )
    exp_size = lax.axis_size("exp")
    band = OV // exp_size
    gathered = lax.all_to_all(
        partial_scores.reshape(exp_size, band, OV), "exp", split_axis=0, concat_axis=0, tiled=True
    )
    scores = jnp.sum(gathered, axis=0)
    row_pos = lax.axis_index("exp") * band + jnp.arange(band, dtype=jnp.int32)[:, None]
    col_pos = jnp.arange(OV, dtype=jnp.int32)[None, :]
    distance = jnp.abs(col_pos - row_pos - offsets[0]).astype(jnp.float32) * (8.0 / OV)
    scores = scores / math.sqrt(D) - distance
    band_weights = jax.nn.softmax(scores, axis=-1).astype(jnp.bfloat16)
    weights = lax.all_to_all(
        jnp.broadcast_to(band_weights[None], (exp_size, band, OV)), "exp", split_axis=0, concat_axis=0, tiled=True
    ).reshape(OV, OV)
    blended = jnp.dot(weights, previous, preferred_element_type=jnp.float32)
    mixed_rows = (0.5 * (head_rows.astype(jnp.float32) + blended)).astype(jnp.bfloat16)
    mixed_rows = jnp.where(lax.axis_index("win") > 0, mixed_rows, head_rows)
    return jnp.concatenate([mixed_rows, layer_state[OV:]], axis=0)


def solution(mesh):
    return jax.shard_map(
        shards,
        mesh=mesh,
        in_specs=(
            P("win", None),
            P(),
            P("win", None, "exp"),
            P("win", "exp", None),
            P("win", None),
            P("win"),
        ),
        out_specs=P("win", "exp"),
        check_vma=False,
    )
```

```python
import math

import jax
import jax.numpy as jnp
from jax import lax
from jax.sharding import PartitionSpec as P

D = 2048
EXPERTS = 32
OV = 256
CAP = 48


def shifted(shard, axis, by):
    count = lax.axis_size(axis)
    pairs = [(i, i + by) for i in range(count) if 0 <= i + by < count]
    return lax.ppermute(shard, axis, pairs)


def ring_reduce(rows, weight, axis, step, half):
    count = lax.axis_size(axis)
    me = lax.axis_index(axis)
    perm = [(i, (i + step) % count) for i in range(count)]
    part = 0 if step > 0 else 1

    def take(k):
        block = (me - step * k + 2 * count) % count
        cols = lax.dynamic_slice_in_dim(weight, (block * 2 + part) * half, half, axis=1)
        return jnp.dot(rows, cols, preferred_element_type=jnp.float32)

    acc = take(1)
    for k in range(count - 1):
        recv = lax.ppermute(acc.astype(jnp.bfloat16), axis, perm)
        acc = recv.astype(jnp.float32) + take(k + 2)
    return acc


def tree_sum(x, axis):
    count = lax.axis_size(axis)
    span = 1
    while span < count:
        x = x + lax.ppermute(x, axis, [(i, i ^ span) for i in range(count)])
        span *= 2
    return x


def shards(tokens, router, w_in, w_out, expert_ids, offsets):
    tok_count = tokens.shape[0]
    win_size = lax.axis_size("win")
    exp_size = lax.axis_size("exp")
    local_experts = w_in.shape[0]
    col_width = D // exp_size
    flat_ids = expert_ids.reshape(-1)
    expert_order = jnp.arange(EXPERTS, dtype=jnp.int32)
    hit_table = (flat_ids[:, None] == expert_order[None, :]).astype(jnp.bfloat16)
    choice_pos = jnp.arange(flat_ids.shape[0], dtype=jnp.int32)
    lower = (choice_pos[:, None] >= choice_pos[None, :]).astype(jnp.bfloat16)
    rank_table = jnp.dot(lower, hit_table, preferred_element_type=jnp.float32)
    slot_index = (jnp.sum(hit_table.astype(jnp.float32) * rank_table, axis=1) - 1.0).astype(jnp.int32)
    slot_target = flat_ids * CAP + slot_index
    slot_pairs = slot_target.reshape(tok_count, 2)
    slot_order = jnp.arange(EXPERTS * CAP, dtype=jnp.int32)[None, :]
    chooser = ((slot_pairs[:, 0:1] == slot_order) | (slot_pairs[:, 1:2] == slot_order)).astype(tokens.dtype)
    split = D // 2
    lane = (D - split) // exp_size
    me_exp = lax.axis_index("exp")
    wide = jnp.einsum("ts,td->sd", chooser, tokens[:, :split], preferred_element_type=jnp.float32)
    wide = wide.astype(tokens.dtype).reshape(win_size, local_experts, CAP, split)
    own_lane = lax.dynamic_slice_in_dim(tokens, split + me_exp * lane, lane, 1)
    narrow = jnp.einsum("ts,td->sd", chooser, own_lane, preferred_element_type=jnp.float32)
    narrow = narrow.astype(tokens.dtype).reshape(win_size, local_experts, CAP, lane)
    narrow = lax.all_to_all(narrow, "win", split_axis=0, concat_axis=0, tiled=True)
    narrow = narrow.reshape(win_size * local_experts * CAP, lane)
    first_proj = w_in.reshape(D, w_in.shape[-1])
    lanes = [(me_exp, narrow)]
    ahead, behind = narrow, narrow
    fwd = [(i, (i + 1) % exp_size) for i in range(exp_size)]
    bwd = [(i, (i - 1) % exp_size) for i in range(exp_size)]
    for k in range(1, exp_size // 2 + 1):
        ahead = lax.ppermute(ahead, "exp", fwd)
        lanes.append(((me_exp - k + exp_size) % exp_size, ahead))
        if k < exp_size - exp_size // 2:
            behind = lax.ppermute(behind, "exp", bwd)
            lanes.append(((me_exp + k) % exp_size, behind))
    wide = lax.all_to_all(wide, "win", split_axis=0, concat_axis=0, tiled=True)
    wide, ahead, behind = lax.optimization_barrier((wide, ahead, behind))
    lanes[-2] = (lanes[-2][0], behind)
    lanes[-1] = (lanes[-1][0], ahead)
    rows_wide = wide.reshape(win_size * local_experts * CAP, split)
    hidden_acc = jnp.dot(rows_wide, first_proj[:split], preferred_element_type=jnp.float32)
    for block, piece in lanes:
        proj = lax.dynamic_slice_in_dim(first_proj, split + block * lane, lane, 0)
        hidden_acc = hidden_acc + jnp.dot(piece, proj, preferred_element_type=jnp.float32)
    hidden_rows = jax.nn.relu(hidden_acc).astype(jnp.bfloat16)
    half = col_width // 2
    rows = hidden_rows
    weight = w_out.reshape(w_out.shape[-2], D)
    reduced = jnp.concatenate(
        [ring_reduce(rows, weight, "exp", 1, half), ring_reduce(rows, weight, "exp", -1, half)], axis=-1
    )
    reduced = reduced.reshape(win_size, local_experts * CAP, col_width)
    returned = lax.all_to_all(reduced, "win", split_axis=0, concat_axis=0, tiled=True)
    logits = jnp.dot(tokens, router, preferred_element_type=jnp.float32)
    first_hit = expert_ids[:, 0:1] == expert_order[None, :]
    second_hit = expert_ids[:, 1:2] == expert_order[None, :]
    logit_first = jnp.sum(jnp.where(first_hit, logits, 0.0), axis=1, keepdims=True)
    logit_second = jnp.sum(jnp.where(second_hit, logits, 0.0), axis=1, keepdims=True)
    gate_first = jax.nn.sigmoid(logit_first - logit_second)
    gate_second = jax.nn.sigmoid(logit_second - logit_first)
    flat_rows = returned.reshape(EXPERTS * CAP, col_width)
    picked = flat_rows[slot_target].reshape(tok_count, 2, col_width)
    expert_sum = gate_first * picked[:, 0] + gate_second * picked[:, 1]
    own_cols = lax.dynamic_slice_in_dim(tokens, lax.axis_index("exp") * col_width, col_width, 1)
    layer_state = (own_cols.astype(jnp.float32) + expert_sum).astype(jnp.bfloat16)
    head_rows = layer_state[:OV]
    tail_rows = layer_state[tok_count - OV :]
    previous = shifted(tail_rows, "win", 1)
    contract = (((1,), (1,)), ((), ()))
    partial_scores = lax.dot_general(
        head_rows, previous, contract, preferred_element_type=jnp.float32
    )
    exp_size = lax.axis_size("exp")
    band = OV // exp_size
    gathered = lax.all_to_all(
        partial_scores.reshape(exp_size, band, OV), "exp", split_axis=0, concat_axis=0, tiled=True
    )
    scores = jnp.sum(gathered, axis=0)
    row_pos = lax.axis_index("exp") * band + jnp.arange(band, dtype=jnp.int32)[:, None]
    col_pos = jnp.arange(OV, dtype=jnp.int32)[None, :]
    distance = jnp.abs(col_pos - row_pos - offsets[0]).astype(jnp.float32) * (8.0 / OV)
    scores = scores / math.sqrt(D) - distance
    band_weights = jax.nn.softmax(scores, axis=-1).astype(jnp.bfloat16)
    weights = lax.all_to_all(
        jnp.broadcast_to(band_weights[None], (exp_size, band, OV)), "exp", split_axis=0, concat_axis=0, tiled=True
    ).reshape(OV, OV)
    blended = jnp.dot(weights, previous, preferred_element_type=jnp.float32)
    mixed_rows = (0.5 * (head_rows.astype(jnp.float32) + blended)).astype(jnp.bfloat16)
    mixed_rows = jnp.where(lax.axis_index("win") > 0, mixed_rows, head_rows)
    return jnp.concatenate([mixed_rows, layer_state[OV:]], axis=0)


def solution(mesh):
    return jax.shard_map(
        shards,
        mesh=mesh,
        in_specs=(
            P("win", None),
            P(),
            P("win", None, "exp"),
            P("win", "exp", None),
            P("win", None),
            P("win"),
        ),
        out_specs=P("win", "exp"),
        check_vma=False,
    )
```

```python
import math

import jax
import jax.numpy as jnp
from jax import lax
from jax.sharding import PartitionSpec as P

D = 2048
EXPERTS = 32
OV = 256
CAP = 48


def shifted(shard, axis, by):
    count = lax.axis_size(axis)
    pairs = [(i, i + by) for i in range(count) if 0 <= i + by < count]
    return lax.ppermute(shard, axis, pairs)


def ring_reduce(rows, weight, axis, step, half):
    count = lax.axis_size(axis)
    me = lax.axis_index(axis)
    perm = [(i, (i + step) % count) for i in range(count)]
    part = 0 if step > 0 else 1

    def take(k):
        block = (me - step * k + 2 * count) % count
        cols = lax.dynamic_slice_in_dim(weight, (block * 2 + part) * half, half, axis=1)
        return jnp.dot(rows, cols, preferred_element_type=jnp.float32)

    acc = take(1)
    for k in range(count - 1):
        recv = lax.ppermute(acc.astype(jnp.bfloat16), axis, perm)
        acc = recv.astype(jnp.float32) + take(k + 2)
    return acc


def tree_sum(x, axis):
    count = lax.axis_size(axis)
    span = 1
    while span < count:
        x = x + lax.ppermute(x, axis, [(i, i ^ span) for i in range(count)])
        span *= 2
    return x


def shards(tokens, router, w_in, w_out, expert_ids, offsets):
    tok_count = tokens.shape[0]
    win_size = lax.axis_size("win")
    exp_size = lax.axis_size("exp")
    local_experts = w_in.shape[0]
    col_width = D // exp_size
    flat_ids = expert_ids.reshape(-1)
    expert_order = jnp.arange(EXPERTS, dtype=jnp.int32)
    hit_table = (flat_ids[:, None] == expert_order[None, :]).astype(jnp.bfloat16)
    choice_pos = jnp.arange(flat_ids.shape[0], dtype=jnp.int32)
    lower = (choice_pos[:, None] >= choice_pos[None, :]).astype(jnp.bfloat16)
    rank_table = jnp.dot(lower, hit_table, preferred_element_type=jnp.float32)
    slot_index = (jnp.sum(hit_table.astype(jnp.float32) * rank_table, axis=1) - 1.0).astype(jnp.int32)
    slot_target = flat_ids * CAP + slot_index
    slot_pairs = slot_target.reshape(tok_count, 2)
    slot_order = jnp.arange(EXPERTS * CAP, dtype=jnp.int32)[None, :]
    chooser = ((slot_pairs[:, 0:1] == slot_order) | (slot_pairs[:, 1:2] == slot_order)).astype(tokens.dtype)
    split = D // 2
    lane = (D - split) // exp_size
    me_exp = lax.axis_index("exp")
    wide = jnp.einsum("ts,td->sd", chooser, tokens[:, :split], preferred_element_type=jnp.float32)
    wide = wide.astype(tokens.dtype).reshape(win_size, local_experts, CAP, split)
    own_lane = lax.dynamic_slice_in_dim(tokens, split + me_exp * lane, lane, 1)
    narrow = jnp.einsum("ts,td->sd", chooser, own_lane, preferred_element_type=jnp.float32)
    narrow = narrow.astype(tokens.dtype).reshape(win_size, local_experts, CAP, lane)
    narrow = lax.all_to_all(narrow, "win", split_axis=0, concat_axis=0, tiled=True)
    narrow = narrow.reshape(win_size * local_experts * CAP, lane)
    first_proj = w_in.reshape(D, w_in.shape[-1])
    lanes = [(me_exp, narrow)]
    ahead, behind = narrow, narrow
    fwd = [(i, (i + 1) % exp_size) for i in range(exp_size)]
    bwd = [(i, (i - 1) % exp_size) for i in range(exp_size)]
    for k in range(1, exp_size // 2 + 1):
        ahead = lax.ppermute(ahead, "exp", fwd)
        lanes.append(((me_exp - k + exp_size) % exp_size, ahead))
        if k < exp_size - exp_size // 2:
            behind = lax.ppermute(behind, "exp", bwd)
            lanes.append(((me_exp + k) % exp_size, behind))
    wide = lax.all_to_all(wide, "win", split_axis=0, concat_axis=0, tiled=True)
    wide, ahead, behind = lax.optimization_barrier((wide, ahead, behind))
    lanes[-2] = (lanes[-2][0], behind)
    lanes[-1] = (lanes[-1][0], ahead)
    rows_all = jnp.concatenate(
        [wide.reshape(win_size * local_experts * CAP, split)] + [piece for _, piece in lanes], axis=1
    )
    proj_all = jnp.concatenate(
        [first_proj[:split]]
        + [lax.dynamic_slice_in_dim(first_proj, split + block * lane, lane, 0) for block, _ in lanes],
        axis=0,
    )
    hidden_acc = jnp.dot(rows_all, proj_all, preferred_element_type=jnp.float32)
    hidden_rows = jax.nn.relu(hidden_acc).astype(jnp.bfloat16)
    half = col_width // 2
    rows = hidden_rows
    weight = w_out.reshape(w_out.shape[-2], D)
    reduced = jnp.concatenate(
        [ring_reduce(rows, weight, "exp", 1, half), ring_reduce(rows, weight, "exp", -1, half)], axis=-1
    )
    reduced = reduced.reshape(win_size, local_experts * CAP, col_width)
    returned = lax.all_to_all(reduced, "win", split_axis=0, concat_axis=0, tiled=True)
    logits = jnp.dot(tokens, router, preferred_element_type=jnp.float32)
    first_hit = expert_ids[:, 0:1] == expert_order[None, :]
    second_hit = expert_ids[:, 1:2] == expert_order[None, :]
    logit_first = jnp.sum(jnp.where(first_hit, logits, 0.0), axis=1, keepdims=True)
    logit_second = jnp.sum(jnp.where(second_hit, logits, 0.0), axis=1, keepdims=True)
    gate_first = jax.nn.sigmoid(logit_first - logit_second)
    gate_second = jax.nn.sigmoid(logit_second - logit_first)
    flat_rows = returned.reshape(EXPERTS * CAP, col_width)
    picked = flat_rows[slot_target].reshape(tok_count, 2, col_width)
    expert_sum = gate_first * picked[:, 0] + gate_second * picked[:, 1]
    own_cols = lax.dynamic_slice_in_dim(tokens, lax.axis_index("exp") * col_width, col_width, 1)
    layer_state = (own_cols.astype(jnp.float32) + expert_sum).astype(jnp.bfloat16)
    head_rows = layer_state[:OV]
    tail_rows = layer_state[tok_count - OV :]
    previous = shifted(tail_rows, "win", 1)
    contract = (((1,), (1,)), ((), ()))
    partial_scores = lax.dot_general(
        head_rows, previous, contract, preferred_element_type=jnp.float32
    )
    exp_size = lax.axis_size("exp")
    band = OV // exp_size
    gathered = lax.all_to_all(
        partial_scores.reshape(exp_size, band, OV), "exp", split_axis=0, concat_axis=0, tiled=True
    )
    scores = jnp.sum(gathered, axis=0)
    row_pos = lax.axis_index("exp") * band + jnp.arange(band, dtype=jnp.int32)[:, None]
    col_pos = jnp.arange(OV, dtype=jnp.int32)[None, :]
    distance = jnp.abs(col_pos - row_pos - offsets[0]).astype(jnp.float32) * (8.0 / OV)
    scores = scores / math.sqrt(D) - distance
    band_weights = jax.nn.softmax(scores, axis=-1).astype(jnp.bfloat16)
    weights = lax.all_to_all(
        jnp.broadcast_to(band_weights[None], (exp_size, band, OV)), "exp", split_axis=0, concat_axis=0, tiled=True
    ).reshape(OV, OV)
    blended = jnp.dot(weights, previous, preferred_element_type=jnp.float32)
    mixed_rows = (0.5 * (head_rows.astype(jnp.float32) + blended)).astype(jnp.bfloat16)
    mixed_rows = jnp.where(lax.axis_index("win") > 0, mixed_rows, head_rows)
    return jnp.concatenate([mixed_rows, layer_state[OV:]], axis=0)


def solution(mesh):
    return jax.shard_map(
        shards,
        mesh=mesh,
        in_specs=(
            P("win", None),
            P(),
            P("win", None, "exp"),
            P("win", "exp", None),
            P("win", None),
            P("win"),
        ),
        out_specs=P("win", "exp"),
        check_vma=False,
    )
```

```python
import math

import jax
import jax.numpy as jnp
from jax import lax
from jax.sharding import PartitionSpec as P

D = 2048
EXPERTS = 32
OV = 256
CAP = 48


def shifted(shard, axis, by):
    count = lax.axis_size(axis)
    pairs = [(i, i + by) for i in range(count) if 0 <= i + by < count]
    return lax.ppermute(shard, axis, pairs)


def ring_reduce(rows, weight, axis, half):
    count = lax.axis_size(axis)
    me = lax.axis_index(axis)
    ahead = [(i, (i + 1) % count) for i in range(count)]
    behind = [(i, (i - 1) % count) for i in range(count)]

    def take(k):
        first = (me - k + 2 * count) % count
        second = (me + k) % count
        cols = jnp.concatenate(
            [
                lax.dynamic_slice_in_dim(weight, first * 2 * half, half, axis=1),
                lax.dynamic_slice_in_dim(weight, (second * 2 + 1) * half, half, axis=1),
            ],
            axis=1,
        )
        both = jnp.dot(rows, cols, preferred_element_type=jnp.float32)
        return both[:, :half], both[:, half:]

    up, down = take(1)
    for k in range(count - 1):
        got_up = lax.ppermute(up.astype(jnp.bfloat16), axis, ahead)
        got_down = lax.ppermute(down.astype(jnp.bfloat16), axis, behind)
        next_up, next_down = take(k + 2)
        up = got_up.astype(jnp.float32) + next_up
        down = got_down.astype(jnp.float32) + next_down
    return jnp.concatenate([up, down], axis=-1)


def tree_sum(x, axis):
    count = lax.axis_size(axis)
    span = 1
    while span < count:
        x = x + lax.ppermute(x, axis, [(i, i ^ span) for i in range(count)])
        span *= 2
    return x


def shards(tokens, router, w_in, w_out, expert_ids, offsets):
    tok_count = tokens.shape[0]
    win_size = lax.axis_size("win")
    exp_size = lax.axis_size("exp")
    local_experts = w_in.shape[0]
    col_width = D // exp_size
    flat_ids = expert_ids.reshape(-1)
    expert_order = jnp.arange(EXPERTS, dtype=jnp.int32)
    hit_table = (flat_ids[:, None] == expert_order[None, :]).astype(jnp.bfloat16)
    choice_pos = jnp.arange(flat_ids.shape[0], dtype=jnp.int32)
    lower = (choice_pos[:, None] >= choice_pos[None, :]).astype(jnp.bfloat16)
    rank_table = jnp.dot(lower, hit_table, preferred_element_type=jnp.float32)
    slot_index = (jnp.sum(hit_table.astype(jnp.float32) * rank_table, axis=1) - 1.0).astype(jnp.int32)
    slot_target = flat_ids * CAP + slot_index
    slot_pairs = slot_target.reshape(tok_count, 2)
    slot_order = jnp.arange(EXPERTS * CAP, dtype=jnp.int32)[None, :]
    chooser = ((slot_pairs[:, 0:1] == slot_order) | (slot_pairs[:, 1:2] == slot_order)).astype(tokens.dtype)
    split = D // 2
    lane = (D - split) // exp_size
    me_exp = lax.axis_index("exp")
    wide = jnp.einsum("ts,td->sd", chooser, tokens[:, :split], preferred_element_type=jnp.float32)
    wide = wide.astype(tokens.dtype).reshape(win_size, local_experts, CAP, split)
    own_lane = lax.dynamic_slice_in_dim(tokens, split + me_exp * lane, lane, 1)
    narrow = jnp.einsum("ts,td->sd", chooser, own_lane, preferred_element_type=jnp.float32)
    narrow = narrow.astype(tokens.dtype).reshape(win_size, local_experts, CAP, lane)
    narrow = lax.all_to_all(narrow, "win", split_axis=0, concat_axis=0, tiled=True)
    narrow = narrow.reshape(win_size * local_experts * CAP, lane)
    first_proj = w_in.reshape(D, w_in.shape[-1])
    lanes = [(me_exp, narrow)]
    ahead, behind = narrow, narrow
    fwd = [(i, (i + 1) % exp_size) for i in range(exp_size)]
    bwd = [(i, (i - 1) % exp_size) for i in range(exp_size)]
    for k in range(1, exp_size // 2 + 1):
        ahead = lax.ppermute(ahead, "exp", fwd)
        lanes.append(((me_exp - k + exp_size) % exp_size, ahead))
        if k < exp_size - exp_size // 2:
            behind = lax.ppermute(behind, "exp", bwd)
            lanes.append(((me_exp + k) % exp_size, behind))
    wide = lax.all_to_all(wide, "win", split_axis=0, concat_axis=0, tiled=True)
    wide, ahead, behind = lax.optimization_barrier((wide, ahead, behind))
    lanes[-2] = (lanes[-2][0], behind)
    lanes[-1] = (lanes[-1][0], ahead)
    rows_all = jnp.concatenate(
        [wide.reshape(win_size * local_experts * CAP, split)] + [piece for _, piece in lanes], axis=1
    )
    proj_all = jnp.concatenate(
        [first_proj[:split]]
        + [lax.dynamic_slice_in_dim(first_proj, split + block * lane, lane, 0) for block, _ in lanes],
        axis=0,
    )
    hidden_acc = jnp.dot(rows_all, proj_all, preferred_element_type=jnp.float32)
    hidden_rows = jax.nn.relu(hidden_acc).astype(jnp.bfloat16)
    half = col_width // 2
    rows = hidden_rows
    weight = w_out.reshape(w_out.shape[-2], D)
    reduced = ring_reduce(rows, weight, "exp", half).astype(jnp.bfloat16)
    reduced = reduced.reshape(win_size, local_experts * CAP, col_width)
    returned = lax.all_to_all(reduced, "win", split_axis=0, concat_axis=0, tiled=True)
    logits = jnp.dot(tokens, router, preferred_element_type=jnp.float32)
    first_hit = expert_ids[:, 0:1] == expert_order[None, :]
    second_hit = expert_ids[:, 1:2] == expert_order[None, :]
    logit_first = jnp.sum(jnp.where(first_hit, logits, 0.0), axis=1, keepdims=True)
    logit_second = jnp.sum(jnp.where(second_hit, logits, 0.0), axis=1, keepdims=True)
    gate_first = jax.nn.sigmoid(logit_first - logit_second)
    gate_second = jax.nn.sigmoid(logit_second - logit_first)
    flat_rows = returned.reshape(EXPERTS * CAP, col_width).astype(jnp.float32)
    picked = flat_rows[slot_target].reshape(tok_count, 2, col_width)
    expert_sum = gate_first * picked[:, 0] + gate_second * picked[:, 1]
    own_cols = lax.dynamic_slice_in_dim(tokens, lax.axis_index("exp") * col_width, col_width, 1)
    layer_state = (own_cols.astype(jnp.float32) + expert_sum).astype(jnp.bfloat16)
    head_rows = layer_state[:OV]
    tail_rows = layer_state[tok_count - OV :]
    previous = shifted(tail_rows, "win", 1)
    contract = (((1,), (1,)), ((), ()))
    partial_scores = lax.dot_general(
        head_rows, previous, contract, preferred_element_type=jnp.float32
    )
    exp_size = lax.axis_size("exp")
    band = OV // exp_size
    gathered = lax.all_to_all(
        partial_scores.astype(jnp.bfloat16).reshape(exp_size, band, OV), "exp", split_axis=0, concat_axis=0, tiled=True
    )
    scores = jnp.sum(gathered.astype(jnp.float32), axis=0)
    row_pos = lax.axis_index("exp") * band + jnp.arange(band, dtype=jnp.int32)[:, None]
    col_pos = jnp.arange(OV, dtype=jnp.int32)[None, :]
    distance = jnp.abs(col_pos - row_pos - offsets[0]).astype(jnp.float32) * (8.0 / OV)
    scores = scores / math.sqrt(D) - distance
    band_weights = jax.nn.softmax(scores, axis=-1).astype(jnp.bfloat16)
    weights = lax.all_to_all(
        jnp.broadcast_to(band_weights[None], (exp_size, band, OV)), "exp", split_axis=0, concat_axis=0, tiled=True
    ).reshape(OV, OV)
    blended = jnp.dot(weights, previous, preferred_element_type=jnp.float32)
    mixed_rows = (0.5 * (head_rows.astype(jnp.float32) + blended)).astype(jnp.bfloat16)
    mixed_rows = jnp.where(lax.axis_index("win") > 0, mixed_rows, head_rows)
    return jnp.concatenate([mixed_rows, layer_state[OV:]], axis=0)


def solution(mesh):
    return jax.shard_map(
        shards,
        mesh=mesh,
        in_specs=(
            P("win", None),
            P(),
            P("win", None, "exp"),
            P("win", "exp", None),
            P("win", None),
            P("win"),
        ),
        out_specs=P("win", "exp"),
        check_vma=False,
    )
```

```python
import math

import jax
import jax.numpy as jnp
from jax import lax
from jax.sharding import PartitionSpec as P

D = 2048
EXPERTS = 32
OV = 256
CAP = 48


def shifted(shard, axis, by):
    count = lax.axis_size(axis)
    pairs = [(i, i + by) for i in range(count) if 0 <= i + by < count]
    return lax.ppermute(shard, axis, pairs)


def ring_reduce(rows, weight, axis, half):
    count = lax.axis_size(axis)
    me = lax.axis_index(axis)
    ahead = [(i, (i + 1) % count) for i in range(count)]
    behind = [(i, (i - 1) % count) for i in range(count)]

    def take(k):
        first = (me - k + 2 * count) % count
        second = (me + k) % count
        cols = jnp.concatenate(
            [
                lax.dynamic_slice_in_dim(weight, first * 2 * half, half, axis=1),
                lax.dynamic_slice_in_dim(weight, (second * 2 + 1) * half, half, axis=1),
            ],
            axis=1,
        )
        both = jnp.dot(rows, cols, preferred_element_type=jnp.float32)
        return both[:, :half], both[:, half:]

    up, down = take(1)
    for k in range(count - 1):
        got_up = lax.ppermute(up.astype(jnp.bfloat16), axis, ahead)
        got_down = lax.ppermute(down.astype(jnp.bfloat16), axis, behind)
        next_up, next_down = take(k + 2)
        up = got_up.astype(jnp.float32) + next_up
        down = got_down.astype(jnp.float32) + next_down
    return jnp.concatenate([up, down], axis=-1)


def tree_sum(x, axis):
    count = lax.axis_size(axis)
    span = 1
    while span < count:
        x = x + lax.ppermute(x, axis, [(i, i ^ span) for i in range(count)])
        span *= 2
    return x


def shards(tokens, router, w_in, w_out, expert_ids, offsets):
    tok_count = tokens.shape[0]
    win_size = lax.axis_size("win")
    exp_size = lax.axis_size("exp")
    local_experts = w_in.shape[0]
    col_width = D // exp_size
    flat_ids = expert_ids.reshape(-1)
    expert_order = jnp.arange(EXPERTS, dtype=jnp.int32)
    hit_table = (flat_ids[:, None] == expert_order[None, :]).astype(jnp.bfloat16)
    choice_pos = jnp.arange(flat_ids.shape[0], dtype=jnp.int32)
    lower = (choice_pos[:, None] >= choice_pos[None, :]).astype(jnp.bfloat16)
    rank_table = jnp.dot(lower, hit_table, preferred_element_type=jnp.float32)
    slot_index = (jnp.sum(hit_table.astype(jnp.float32) * rank_table, axis=1) - 1.0).astype(jnp.int32)
    slot_target = flat_ids * CAP + slot_index
    slot_pairs = slot_target.reshape(tok_count, 2)
    slot_order = jnp.arange(EXPERTS * CAP, dtype=jnp.int32)[None, :]
    chooser = ((slot_pairs[:, 0:1] == slot_order) | (slot_pairs[:, 1:2] == slot_order)).astype(tokens.dtype)
    split = D // 2
    lane = (D - split) // exp_size
    me_exp = lax.axis_index("exp")
    wide = jnp.einsum("ts,td->sd", chooser, tokens[:, :split], preferred_element_type=jnp.float32)
    wide = wide.astype(tokens.dtype).reshape(win_size, local_experts, CAP, split)
    own_lane = lax.dynamic_slice_in_dim(tokens, split + me_exp * lane, lane, 1)
    narrow = jnp.einsum("ts,td->sd", chooser, own_lane, preferred_element_type=jnp.float32)
    narrow = narrow.astype(tokens.dtype).reshape(win_size, local_experts, CAP, lane)
    narrow = lax.all_to_all(narrow, "win", split_axis=0, concat_axis=0, tiled=True)
    narrow = narrow.reshape(win_size * local_experts * CAP, lane)
    first_proj = w_in.reshape(D, w_in.shape[-1])
    lanes = [(me_exp, narrow)]
    ahead, behind = narrow, narrow
    fwd = [(i, (i + 1) % exp_size) for i in range(exp_size)]
    bwd = [(i, (i - 1) % exp_size) for i in range(exp_size)]
    for k in range(1, exp_size // 2 + 1):
        ahead = lax.ppermute(ahead, "exp", fwd)
        lanes.append(((me_exp - k + exp_size) % exp_size, ahead))
        if k < exp_size - exp_size // 2:
            behind = lax.ppermute(behind, "exp", bwd)
            lanes.append(((me_exp + k) % exp_size, behind))
    wide = lax.all_to_all(wide, "win", split_axis=0, concat_axis=0, tiled=True)
    wide, ahead, behind = lax.optimization_barrier((wide, ahead, behind))
    lanes[-2] = (lanes[-2][0], behind)
    lanes[-1] = (lanes[-1][0], ahead)
    narrow_all = jnp.zeros((win_size * local_experts * CAP, D - split), tokens.dtype)
    for block, piece in lanes:
        narrow_all = lax.dynamic_update_slice_in_dim(narrow_all, piece, block * lane, axis=1)
    rows_all = jnp.concatenate([wide.reshape(win_size * local_experts * CAP, split), narrow_all], axis=1)
    proj_all = first_proj
    hidden_acc = jnp.dot(rows_all, proj_all, preferred_element_type=jnp.float32)
    hidden_rows = jax.nn.relu(hidden_acc).astype(jnp.bfloat16)
    half = col_width // 2
    rows = hidden_rows
    weight = w_out.reshape(w_out.shape[-2], D)
    reduced = ring_reduce(rows, weight, "exp", half).astype(jnp.bfloat16)
    reduced = reduced.reshape(win_size, local_experts * CAP, col_width)
    returned = lax.all_to_all(reduced, "win", split_axis=0, concat_axis=0, tiled=True)
    logits = jnp.dot(tokens, router, preferred_element_type=jnp.float32)
    first_hit = expert_ids[:, 0:1] == expert_order[None, :]
    second_hit = expert_ids[:, 1:2] == expert_order[None, :]
    logit_first = jnp.sum(jnp.where(first_hit, logits, 0.0), axis=1, keepdims=True)
    logit_second = jnp.sum(jnp.where(second_hit, logits, 0.0), axis=1, keepdims=True)
    gate_first = jax.nn.sigmoid(logit_first - logit_second)
    gate_second = jax.nn.sigmoid(logit_second - logit_first)
    flat_rows = returned.reshape(EXPERTS * CAP, col_width).astype(jnp.float32)
    picked = flat_rows[slot_target].reshape(tok_count, 2, col_width)
    expert_sum = gate_first * picked[:, 0] + gate_second * picked[:, 1]
    own_cols = lax.dynamic_slice_in_dim(tokens, lax.axis_index("exp") * col_width, col_width, 1)
    layer_state = (own_cols.astype(jnp.float32) + expert_sum).astype(jnp.bfloat16)
    head_rows = layer_state[:OV]
    tail_rows = layer_state[tok_count - OV :]
    previous = shifted(tail_rows, "win", 1)
    contract = (((1,), (1,)), ((), ()))
    partial_scores = lax.dot_general(
        head_rows, previous, contract, preferred_element_type=jnp.float32
    )
    exp_size = lax.axis_size("exp")
    band = OV // exp_size
    gathered = lax.all_to_all(
        partial_scores.astype(jnp.bfloat16).reshape(exp_size, band, OV), "exp", split_axis=0, concat_axis=0, tiled=True
    )
    scores = jnp.sum(gathered.astype(jnp.float32), axis=0)
    row_pos = lax.axis_index("exp") * band + jnp.arange(band, dtype=jnp.int32)[:, None]
    col_pos = jnp.arange(OV, dtype=jnp.int32)[None, :]
    distance = jnp.abs(col_pos - row_pos - offsets[0]).astype(jnp.float32) * (8.0 / OV)
    scores = scores / math.sqrt(D) - distance
    band_weights = jax.nn.softmax(scores, axis=-1).astype(jnp.bfloat16)
    weights = lax.all_to_all(
        jnp.broadcast_to(band_weights[None], (exp_size, band, OV)), "exp", split_axis=0, concat_axis=0, tiled=True
    ).reshape(OV, OV)
    blended = jnp.dot(weights, previous, preferred_element_type=jnp.float32)
    mixed_rows = (0.5 * (head_rows.astype(jnp.float32) + blended)).astype(jnp.bfloat16)
    mixed_rows = jnp.where(lax.axis_index("win") > 0, mixed_rows, head_rows)
    return jnp.concatenate([mixed_rows, layer_state[OV:]], axis=0)


def solution(mesh):
    return jax.shard_map(
        shards,
        mesh=mesh,
        in_specs=(
            P("win", None),
            P(),
            P("win", None, "exp"),
            P("win", "exp", None),
            P("win", None),
            P("win"),
        ),
        out_specs=P("win", "exp"),
        check_vma=False,
    )
```

```python
import math

import jax
import jax.numpy as jnp
from jax import lax
from jax.sharding import PartitionSpec as P

D = 2048
EXPERTS = 32
OV = 256
CAP = 48


def shifted(shard, axis, by):
    count = lax.axis_size(axis)
    pairs = [(i, i + by) for i in range(count) if 0 <= i + by < count]
    return lax.ppermute(shard, axis, pairs)


def ring_reduce(rows, weight, axis, half):
    count = lax.axis_size(axis)
    me = lax.axis_index(axis)
    ahead = [(i, (i + 1) % count) for i in range(count)]
    behind = [(i, (i - 1) % count) for i in range(count)]

    def take(k):
        first = (me - k + 2 * count) % count
        second = (me + k) % count
        cols = jnp.concatenate(
            [
                lax.dynamic_slice_in_dim(weight, first * 2 * half, half, axis=1),
                lax.dynamic_slice_in_dim(weight, (second * 2 + 1) * half, half, axis=1),
            ],
            axis=1,
        )
        both = jnp.dot(rows, cols, preferred_element_type=jnp.float32)
        return both[:, :half], both[:, half:]

    up, down = take(1)
    for k in range(count - 1):
        got_up = lax.ppermute(up.astype(jnp.bfloat16), axis, ahead)
        got_down = lax.ppermute(down.astype(jnp.bfloat16), axis, behind)
        next_up, next_down = take(k + 2)
        up = got_up.astype(jnp.float32) + next_up
        down = got_down.astype(jnp.float32) + next_down
    return jnp.concatenate([up, down], axis=-1)


def tree_sum(x, axis):
    count = lax.axis_size(axis)
    span = 1
    while span < count:
        x = x + lax.ppermute(x, axis, [(i, i ^ span) for i in range(count)])
        span *= 2
    return x


def shards(tokens, router, w_in, w_out, expert_ids, offsets):
    tok_count = tokens.shape[0]
    win_size = lax.axis_size("win")
    exp_size = lax.axis_size("exp")
    local_experts = w_in.shape[0]
    col_width = D // exp_size
    flat_ids = expert_ids.reshape(-1)
    expert_order = jnp.arange(EXPERTS, dtype=jnp.int32)
    hit_table = (flat_ids[:, None] == expert_order[None, :]).astype(jnp.bfloat16)
    choice_pos = jnp.arange(flat_ids.shape[0], dtype=jnp.int32)
    lower = (choice_pos[:, None] >= choice_pos[None, :]).astype(jnp.bfloat16)
    rank_table = jnp.dot(lower, hit_table, preferred_element_type=jnp.float32)
    slot_index = (jnp.sum(hit_table.astype(jnp.float32) * rank_table, axis=1) - 1.0).astype(jnp.int32)
    slot_target = flat_ids * CAP + slot_index
    slot_pairs = slot_target.reshape(tok_count, 2)
    slot_order = jnp.arange(EXPERTS * CAP, dtype=jnp.int32)[None, :]
    chooser = ((slot_pairs[:, 0:1] == slot_order) | (slot_pairs[:, 1:2] == slot_order)).astype(tokens.dtype)
    split = D // 2
    lane = (D - split) // exp_size
    me_exp = lax.axis_index("exp")
    wide = jnp.einsum("ts,td->sd", chooser, tokens[:, :split], preferred_element_type=jnp.float32)
    wide = wide.astype(tokens.dtype).reshape(win_size, local_experts, CAP, split)
    own_lane = lax.dynamic_slice_in_dim(tokens, split + me_exp * lane, lane, 1)
    narrow = jnp.einsum("ts,td->sd", chooser, own_lane, preferred_element_type=jnp.float32)
    narrow = narrow.astype(tokens.dtype).reshape(win_size, local_experts, CAP, lane)
    narrow = lax.all_to_all(narrow, "win", split_axis=0, concat_axis=0, tiled=True)
    narrow = narrow.reshape(win_size * local_experts * CAP, lane)
    first_proj = w_in.reshape(D, w_in.shape[-1])
    lanes = [(me_exp, narrow)]
    ahead, behind = narrow, narrow
    fwd = [(i, (i + 1) % exp_size) for i in range(exp_size)]
    bwd = [(i, (i - 1) % exp_size) for i in range(exp_size)]
    for k in range(1, exp_size // 2 + 1):
        ahead = lax.ppermute(ahead, "exp", fwd)
        lanes.append(((me_exp - k + exp_size) % exp_size, ahead))
        if k < exp_size - exp_size // 2:
            behind = lax.ppermute(behind, "exp", bwd)
            lanes.append(((me_exp + k) % exp_size, behind))
    wide = lax.all_to_all(wide, "win", split_axis=0, concat_axis=0, tiled=True)
    wide, ahead, behind = lax.optimization_barrier((wide, ahead, behind))
    lanes[-2] = (lanes[-2][0], behind)
    lanes[-1] = (lanes[-1][0], ahead)
    narrow_all = jnp.zeros((win_size * local_experts * CAP, D - split), tokens.dtype)
    for block, piece in lanes:
        narrow_all = lax.dynamic_update_slice_in_dim(narrow_all, piece, block * lane, axis=1)
    rows_all = jnp.concatenate([wide.reshape(win_size * local_experts * CAP, split), narrow_all], axis=1)
    proj_all = first_proj
    hidden_acc = jnp.dot(rows_all, proj_all, preferred_element_type=jnp.float32)
    hidden_rows = jax.nn.relu(hidden_acc).astype(jnp.bfloat16)
    half = col_width // 2
    rows = hidden_rows
    weight = w_out.reshape(w_out.shape[-2], D)
    reduced = ring_reduce(rows, weight, "exp", half).astype(jnp.bfloat16)
    reduced = reduced.reshape(win_size, local_experts * CAP, col_width)
    returned = lax.all_to_all(reduced, "win", split_axis=0, concat_axis=0, tiled=True)
    logits = jnp.dot(tokens, router, preferred_element_type=jnp.float32)
    first_hit = expert_ids[:, 0:1] == expert_order[None, :]
    second_hit = expert_ids[:, 1:2] == expert_order[None, :]
    logit_first = jnp.sum(jnp.where(first_hit, logits, 0.0), axis=1, keepdims=True)
    logit_second = jnp.sum(jnp.where(second_hit, logits, 0.0), axis=1, keepdims=True)
    gate_first = jax.nn.sigmoid(logit_first - logit_second)
    gate_second = jax.nn.sigmoid(logit_second - logit_first)
    flat_rows = returned.reshape(EXPERTS * CAP, col_width).astype(jnp.float32)
    picked = flat_rows[slot_target].reshape(tok_count, 2, col_width)
    expert_sum = gate_first * picked[:, 0] + gate_second * picked[:, 1]
    own_cols = lax.dynamic_slice_in_dim(tokens, lax.axis_index("exp") * col_width, col_width, 1)
    layer_state = (own_cols.astype(jnp.float32) + expert_sum).astype(jnp.bfloat16)
    head_rows = layer_state[:OV]
    tail_rows = layer_state[tok_count - OV :]
    previous = shifted(tail_rows, "win", 1)
    contract = (((1,), (1,)), ((), ()))
    partial_scores = lax.dot_general(
        head_rows, previous, contract, preferred_element_type=jnp.float32
    )
    exp_size = lax.axis_size("exp")
    gathered = lax.all_to_all(
        jnp.broadcast_to(partial_scores.astype(jnp.bfloat16)[None], (exp_size, OV, OV)),
        "exp",
        split_axis=0,
        concat_axis=0,
        tiled=True,
    )
    scores = jnp.sum(gathered.astype(jnp.float32), axis=0)
    row_pos = jnp.arange(OV, dtype=jnp.int32)[:, None]
    col_pos = jnp.arange(OV, dtype=jnp.int32)[None, :]
    distance = jnp.abs(col_pos - row_pos - offsets[0]).astype(jnp.float32) * (8.0 / OV)
    scores = scores / math.sqrt(D) - distance
    weights = jax.nn.softmax(scores, axis=-1).astype(jnp.bfloat16)
    blended = jnp.dot(weights, previous, preferred_element_type=jnp.float32)
    mixed_rows = (0.5 * (head_rows.astype(jnp.float32) + blended)).astype(jnp.bfloat16)
    mixed_rows = jnp.where(lax.axis_index("win") > 0, mixed_rows, head_rows)
    return jnp.concatenate([mixed_rows, layer_state[OV:]], axis=0)


def solution(mesh):
    return jax.shard_map(
        shards,
        mesh=mesh,
        in_specs=(
            P("win", None),
            P(),
            P("win", None, "exp"),
            P("win", "exp", None),
            P("win", None),
            P("win"),
        ),
        out_specs=P("win", "exp"),
        check_vma=False,
    )
```

```python
import math

import jax
import jax.numpy as jnp
from jax import lax
from jax.sharding import PartitionSpec as P

D = 2048
EXPERTS = 32
OV = 256
CAP = 48


def shifted(shard, axis, by):
    count = lax.axis_size(axis)
    pairs = [(i, i + by) for i in range(count) if 0 <= i + by < count]
    return lax.ppermute(shard, axis, pairs)


def ring_reduce(rows, weight, axis, half):
    count = lax.axis_size(axis)
    me = lax.axis_index(axis)
    ahead = [(i, (i + 1) % count) for i in range(count)]
    behind = [(i, (i - 1) % count) for i in range(count)]

    def take(k):
        first = (me - k + 2 * count) % count
        second = (me + k) % count
        cols = jnp.concatenate(
            [
                lax.dynamic_slice_in_dim(weight, first * 2 * half, half, axis=1),
                lax.dynamic_slice_in_dim(weight, (second * 2 + 1) * half, half, axis=1),
            ],
            axis=1,
        )
        both = jnp.dot(rows, cols, preferred_element_type=jnp.float32)
        return both[:, :half], both[:, half:]

    up, down = take(1)
    for k in range(count - 1):
        got_up = lax.ppermute(up.astype(jnp.bfloat16), axis, ahead)
        got_down = lax.ppermute(down.astype(jnp.bfloat16), axis, behind)
        next_up, next_down = take(k + 2)
        up = got_up.astype(jnp.float32) + next_up
        down = got_down.astype(jnp.float32) + next_down
    return jnp.concatenate([up, down], axis=-1)


def tree_sum(x, axis):
    count = lax.axis_size(axis)
    span = 1
    while span < count:
        x = x + lax.ppermute(x, axis, [(i, i ^ span) for i in range(count)])
        span *= 2
    return x


def shards(tokens, router, w_in, w_out, expert_ids, offsets):
    tok_count = tokens.shape[0]
    win_size = lax.axis_size("win")
    exp_size = lax.axis_size("exp")
    local_experts = w_in.shape[0]
    col_width = D // exp_size
    flat_ids = expert_ids.reshape(-1)
    expert_order = jnp.arange(EXPERTS, dtype=jnp.int32)
    hit_table = (flat_ids[:, None] == expert_order[None, :]).astype(jnp.bfloat16)
    choice_pos = jnp.arange(flat_ids.shape[0], dtype=jnp.int32)
    lower = (choice_pos[:, None] >= choice_pos[None, :]).astype(jnp.bfloat16)
    rank_table = jnp.dot(lower, hit_table, preferred_element_type=jnp.float32)
    slot_index = (jnp.sum(hit_table.astype(jnp.float32) * rank_table, axis=1) - 1.0).astype(jnp.int32)
    slot_target = flat_ids * CAP + slot_index
    slot_pairs = slot_target.reshape(tok_count, 2)
    slot_order = jnp.arange(EXPERTS * CAP, dtype=jnp.int32)[None, :]
    chooser = ((slot_pairs[:, 0:1] == slot_order) | (slot_pairs[:, 1:2] == slot_order)).astype(tokens.dtype)
    split = D // 2
    lane = (D - split) // exp_size
    me_exp = lax.axis_index("exp")
    wide = jnp.einsum("ts,td->sd", chooser, tokens[:, :split], preferred_element_type=jnp.float32)
    wide = wide.astype(tokens.dtype).reshape(win_size, local_experts, CAP, split)
    own_lane = lax.dynamic_slice_in_dim(tokens, split + me_exp * lane, lane, 1)
    narrow = jnp.einsum("ts,td->sd", chooser, own_lane, preferred_element_type=jnp.float32)
    narrow = narrow.astype(tokens.dtype).reshape(win_size, local_experts, CAP, lane)
    narrow = lax.all_to_all(narrow, "win", split_axis=0, concat_axis=0, tiled=True)
    narrow = narrow.reshape(win_size * local_experts * CAP, lane)
    first_proj = w_in.reshape(D, w_in.shape[-1])
    lanes = [(me_exp, narrow)]
    ahead, behind = narrow, narrow
    fwd = [(i, (i + 1) % exp_size) for i in range(exp_size)]
    bwd = [(i, (i - 1) % exp_size) for i in range(exp_size)]
    for k in range(1, exp_size // 2 + 1):
        ahead = lax.ppermute(ahead, "exp", fwd)
        lanes.append(((me_exp - k + exp_size) % exp_size, ahead))
        if k < exp_size - exp_size // 2:
            behind = lax.ppermute(behind, "exp", bwd)
            lanes.append(((me_exp + k) % exp_size, behind))
    wide = lax.all_to_all(wide, "win", split_axis=0, concat_axis=0, tiled=True)
    wide, ahead, behind = lax.optimization_barrier((wide, ahead, behind))
    lanes[-2] = (lanes[-2][0], behind)
    lanes[-1] = (lanes[-1][0], ahead)
    narrow_all = jnp.zeros((win_size * local_experts * CAP, D - split), tokens.dtype)
    for block, piece in lanes:
        narrow_all = lax.dynamic_update_slice_in_dim(narrow_all, piece, block * lane, axis=1)
    rows_all = jnp.concatenate([wide.reshape(win_size * local_experts * CAP, split), narrow_all], axis=1)
    proj_all = first_proj
    hidden_acc = jnp.dot(rows_all, proj_all, preferred_element_type=jnp.float32)
    hidden_rows = jax.nn.relu(hidden_acc).astype(jnp.bfloat16)
    half = col_width // 2
    rows = hidden_rows
    weight = w_out.reshape(w_out.shape[-2], D)
    reduced = ring_reduce(rows, weight, "exp", half).astype(jnp.bfloat16)
    reduced = reduced.reshape(win_size, local_experts * CAP, col_width)
    returned = lax.all_to_all(reduced, "win", split_axis=0, concat_axis=0, tiled=True)
    logits = jnp.dot(tokens, router, preferred_element_type=jnp.float32)
    first_hit = expert_ids[:, 0:1] == expert_order[None, :]
    second_hit = expert_ids[:, 1:2] == expert_order[None, :]
    logit_first = jnp.sum(jnp.where(first_hit, logits, 0.0), axis=1, keepdims=True)
    logit_second = jnp.sum(jnp.where(second_hit, logits, 0.0), axis=1, keepdims=True)
    gate_first = jax.nn.sigmoid(logit_first - logit_second)
    gate_second = jax.nn.sigmoid(logit_second - logit_first)
    flat_rows = returned.reshape(EXPERTS * CAP, col_width)
    every_slot = jnp.arange(EXPERTS * CAP, dtype=jnp.int32)[None, :]
    gate_grid = jnp.where(slot_pairs[:, 0:1] == every_slot, gate_first, 0.0) + jnp.where(
        slot_pairs[:, 1:2] == every_slot, gate_second, 0.0
    )
    grid_hi = gate_grid.astype(jnp.bfloat16)
    grid_lo = (gate_grid - grid_hi.astype(jnp.float32)).astype(jnp.bfloat16)
    expert_sum = jnp.dot(grid_hi, flat_rows, preferred_element_type=jnp.float32) + jnp.dot(
        grid_lo, flat_rows, preferred_element_type=jnp.float32
    )
    own_cols = lax.dynamic_slice_in_dim(tokens, lax.axis_index("exp") * col_width, col_width, 1)
    layer_state = (own_cols.astype(jnp.float32) + expert_sum).astype(jnp.bfloat16)
    head_rows = layer_state[:OV]
    tail_rows = layer_state[tok_count - OV :]
    previous = shifted(tail_rows, "win", 1)
    contract = (((1,), (1,)), ((), ()))
    partial_scores = lax.dot_general(
        head_rows, previous, contract, preferred_element_type=jnp.float32
    )
    exp_size = lax.axis_size("exp")
    band = OV // exp_size
    gathered = lax.all_to_all(
        partial_scores.astype(jnp.bfloat16).reshape(exp_size, band, OV), "exp", split_axis=0, concat_axis=0, tiled=True
    )
    scores = jnp.sum(gathered.astype(jnp.float32), axis=0)
    row_pos = lax.axis_index("exp") * band + jnp.arange(band, dtype=jnp.int32)[:, None]
    col_pos = jnp.arange(OV, dtype=jnp.int32)[None, :]
    distance = jnp.abs(col_pos - row_pos - offsets[0]).astype(jnp.float32) * (8.0 / OV)
    scores = scores / math.sqrt(D) - distance
    band_weights = jax.nn.softmax(scores, axis=-1).astype(jnp.bfloat16)
    weights = lax.all_to_all(
        jnp.broadcast_to(band_weights[None], (exp_size, band, OV)), "exp", split_axis=0, concat_axis=0, tiled=True
    ).reshape(OV, OV)
    blended = jnp.dot(weights, previous, preferred_element_type=jnp.float32)
    mixed_rows = (0.5 * (head_rows.astype(jnp.float32) + blended)).astype(jnp.bfloat16)
    mixed_rows = jnp.where(lax.axis_index("win") > 0, mixed_rows, head_rows)
    return jnp.concatenate([mixed_rows, layer_state[OV:]], axis=0)


def solution(mesh):
    return jax.shard_map(
        shards,
        mesh=mesh,
        in_specs=(
            P("win", None),
            P(),
            P("win", None, "exp"),
            P("win", "exp", None),
            P("win", None),
            P("win"),
        ),
        out_specs=P("win", "exp"),
        check_vma=False,
    )
```
